256 devices in a mesh: row: 16 (over z_lo, x), col: 16 (over y, z_hi, core).
Axes of the slice: x: 4, y: 4, z: 8 (z_hi: 2, z_lo: 4; z = z_hi * 4 + z_lo), core: 2. Of those that a mesh axis runs over, the one named last changes fastest.
Arguments:
- traces: bfloat16 [32768, 1024], P(('row', 'col'))
- alive: int32 [32768], P(('row', 'col')), may hold values 0 or 1
- pair_list: int32 [1024, 2], P(('row', 'col')), may hold values from -1 to 255, as said below
Outputs:
- correlations: bfloat16 [1024, 128, 65, 128], P(('row', 'col'))
The draws below stay inside these ranges and needn't reach their ends.
Inputs may be any that keep to these rules, and one draw needn't show every extreme that they name: `pair_list`: slots p * 4 to (p + 1) * 4 - 1 belong to flat device p = r * 16 + c (r its row index, c its col index); they hold 1 to 4 live pairs first and then (-1, -1) pairs; in every draw some device has all 4 slots live. A live pair (a, b) of that device has a // 16 == r, b % 16 == c and b >= a.
All inputs are finite; a program needn't handle non-finite values. No bound on the sum of `alive` on one device may be relied on, other than what follows from the above.
Results may differ from the reference program's by a relative error of at most 0.0042.
Values may be sent and summed in bfloat16 or wider, within the bound.
No kernel may reach another device: no remote copies, remote signals or barrier semaphores. Data moves between devices by JAX's collectives and lax.ppermute only.
A program may use at most 128 MiB of HBM per device.

```python
import jax
import jax.numpy as jnp
from jax import lax

BLK = 128
LAGS = 65
SAMPLES = 1024
SLOTS = 4
CHANNELS = 32768
N_ROW = 16
N_COL = 16
DEVICES = 256


def draw_traces(key, part):
    keys = jax.random.split(key, 4)
    delays = jax.random.randint(keys[0], (CHANNELS,), 0, (LAGS - 1) // 2)
    source = jax.random.normal(keys[1], (SAMPLES + LAGS,), jnp.float32)
    positions = jnp.arange(SAMPLES)[None, :] + delays[:, None]
    coherent = jnp.take(source, positions)
    amplitude = jnp.exp(jax.random.uniform(keys[3], (CHANNELS, 1), jnp.float32, -1.5, 1.5))
    noise = jax.random.normal(keys[2], (CHANNELS, SAMPLES), jnp.float32)
    mixed = 0.8 * coherent + 0.6 * noise
    return (amplitude * mixed).astype(jnp.bfloat16)


def draw_pair_list(key, part):
    keys = jax.random.split(key, 4)
    device = jnp.arange(DEVICES, dtype=jnp.int32)
    counts = jax.random.randint(keys[0], (DEVICES,), 1, SLOTS + 1)
    fullest = jax.random.randint(keys[1], (), 0, DEVICES)
    counts = jnp.where((device == fullest) | (device == 0), SLOTS, counts)
    row_index = jnp.broadcast_to((device // N_COL)[:, None], (DEVICES, SLOTS))
    col_index = jnp.broadcast_to((device % N_COL)[:, None], (DEVICES, SLOTS))
    target = row_index + jax.random.randint(keys[2], (DEVICES, SLOTS), 0, 1048576) % (N_ROW - row_index)
    slot_index = jnp.broadcast_to(jnp.arange(SLOTS, dtype=jnp.int32)[None, :], (DEVICES, SLOTS))
    forced = jnp.where(slot_index == 0, N_ROW - 1, jnp.where(slot_index == 1, N_ROW // 2, target))
    target = jnp.where(device[:, None] == 0, forced, target)
    highest = jnp.where(target == row_index, col_index + 1, N_COL)
    picked = jax.random.randint(keys[3], (DEVICES, SLOTS), 0, 1048576) % highest
    first = row_index * N_COL + picked
    second = target * N_COL + col_index
    living = slot_index < counts[:, None]
    first = jnp.where(living, first, -1)
    second = jnp.where(living, second, -1)
    return jnp.stack([first, second], axis=-1).reshape(DEVICES * SLOTS, 2).astype(jnp.int32)


def place_ends(array, rng, low, high):
    longest = array.shape.index(max(array.shape))
    spots = []
    for shift in (0, 1):
        where = [jax.random.randint(jax.random.fold_in(rng, axis), (), 0, length) for axis, length in enumerate(array.shape)]
        where[longest] = (where[longest] + shift) % array.shape[longest]
        spots.append(tuple(where))
    return array.at[spots[0]].set(low).at[spots[1]].set(high)


def setup_inputs(seed: int = 0) -> dict:
    key_list = jax.random.split(jax.random.key(seed), 4)
    traces = draw_traces(jax.random.fold_in(key_list[3], 71), 0)
    alive = place_ends((jax.random.randint(key_list[1], (CHANNELS,), 0, 10) < 9).astype(jnp.int32), jax.random.fold_in(key_list[1], 1), 0, 1)
    pair_list = draw_pair_list(jax.random.fold_in(key_list[3], 71), 0)
    return {"traces": traces, "alive": alive, "pair_list": pair_list}


def whiten(traces, alive):
    samples = traces.astype(jnp.float32)
    centered = samples - lax.optimization_barrier(jnp.mean(samples, axis=1, keepdims=True))
    power = lax.optimization_barrier(jnp.mean(centered * centered, axis=1, keepdims=True))
    factor = alive.astype(jnp.float32)[:, None] / jnp.sqrt(power + 1e-05)
    return (centered * factor).astype(jnp.bfloat16)

def correlate(left_block, right_block):
    length = left_block.shape[1]
    width = left_block.shape[0]
    reach = (LAGS - 1) // 2
    padded = jnp.pad(right_block, ((0, 0), (reach, reach)))
    shifted = jnp.stack([padded[:, offset:offset + length] for offset in range(LAGS)], axis=0)
    shifted = shifted.reshape(LAGS * width, length)
    summed = lax.dot_general(left_block, shifted, (((1,), (1,)), ((), ())), preferred_element_type=jnp.float32)
    return (summed * (1.0 / length)).reshape(width, LAGS, width).astype(jnp.bfloat16)

def reference(traces, alive, pair_list):
    whitened = lax.optimization_barrier(whiten(traces, alive)).astype(jnp.float32)

    def one_pair(pair):
        first = pair[0]
        second = pair[1]

        def compute(unused):
            left_block = lax.dynamic_slice_in_dim(whitened, (jnp.maximum(first, 0) * BLK).astype(jnp.int32), BLK, 0)
            right_block = lax.dynamic_slice_in_dim(whitened, (jnp.maximum(second, 0) * BLK).astype(jnp.int32), BLK, 0)
            return correlate(left_block, right_block)

        def empty(unused):
            return jnp.zeros((BLK, LAGS, BLK), jnp.bfloat16)
        return lax.cond(first >= 0, compute, empty, 0)
    return lax.map(one_pair, pair_list)
```

```python
import jax
import jax.numpy as jnp
from jax import lax
from jax.experimental import pallas as pl
from jax.experimental.pallas import tpu as pltpu
from jax.sharding import PartitionSpec as P

LAGS = 65
REACH = (LAGS - 1) // 2
PAD = 64


def whiten(traces, alive):
    samples = traces.astype(jnp.float32)
    centered = samples - jnp.mean(samples, axis=1, keepdims=True)
    power = jnp.mean(centered * centered, axis=1, keepdims=True)
    factor = alive.astype(jnp.float32)[:, None] / jnp.sqrt(power + 1e-05)
    return (centered * factor).astype(jnp.bfloat16)


def correlate_kernel(live_ref, l_ref, r_ref, o_ref):
    slot = pl.program_id(0)
    length = l_ref.shape[2]

    @pl.when(live_ref[slot] > 0)
    def _():
        left = l_ref[0]
        for k in range(LAGS):
            shifted = r_ref[0, :, pl.ds(PAD - REACH + k, length)]
            summed = lax.dot_general(
                left, shifted, (((1,), (1,)), ((), ())), preferred_element_type=jnp.float32
            )
            o_ref[0, k] = (summed * (1.0 / length)).astype(o_ref.dtype)

    @pl.when(live_ref[slot] <= 0)
    def _():
        o_ref[...] = jnp.zeros(o_ref.shape, o_ref.dtype)


def correlate_all(live, left, right):
    slots, width, length = left.shape
    padded = jnp.pad(right, ((0, 0), (0, 0), (PAD, PAD)))
    out = pl.pallas_call(
        correlate_kernel,
        grid_spec=pltpu.PrefetchScalarGridSpec(
            num_scalar_prefetch=1,
            grid=(slots,),
            in_specs=[
                pl.BlockSpec((1, width, length), lambda s, lv: (s, 0, 0)),
                pl.BlockSpec((1, width, length + 2 * PAD), lambda s, lv: (s, 0, 0)),
            ],
            out_specs=pl.BlockSpec((1, LAGS, width, width), lambda s, lv: (s, 0, 0, 0)),
        ),
        out_shape=jax.ShapeDtypeStruct((slots, LAGS, width, width), jnp.bfloat16),
        compiler_params=pltpu.CompilerParams(vmem_limit_bytes=48 * 1024 * 1024),
    )(live, left, padded)
    return jnp.transpose(out, (0, 2, 1, 3))


def shards(traces, alive, pair_list):
    whitened = whiten(traces, alive)
    block = whitened.shape[0]
    across = lax.axis_size("col")
    row_panel = lax.all_gather(whitened, "col", axis=0, tiled=True)
    col_panel = lax.all_gather(whitened, "row", axis=0, tiled=True)
    row_first = lax.axis_index("row") * across
    row_place = jnp.clip(pair_list[:, 0] - row_first, 0, across - 1)
    col_place = jnp.maximum(pair_list[:, 1], 0) // across
    live = (pair_list[:, 0] >= 0).astype(jnp.int32)
    left = jnp.stack(
        [lax.dynamic_slice_in_dim(row_panel, row_place[s] * block, block, 0) for s in range(pair_list.shape[0])]
    )
    right = jnp.stack(
        [lax.dynamic_slice_in_dim(col_panel, col_place[s] * block, block, 0) for s in range(pair_list.shape[0])]
    )
    return correlate_all(live, left, right)


def solution(mesh):
    in_specs = (P(("row", "col"), None), P(("row", "col")), P(("row", "col"), None))
    out_specs = P(("row", "col"), None, None, None)
    return jax.shard_map(shards, mesh=mesh, in_specs=in_specs, out_specs=out_specs, check_vma=False)
```

```python
import jax
import jax.numpy as jnp
from jax import lax
from jax.experimental import pallas as pl
from jax.experimental.pallas import tpu as pltpu
from jax.sharding import PartitionSpec as P

LAGS = 65
REACH = (LAGS - 1) // 2
PAD = 64
META = 128


def whiten(traces, alive):
    samples = traces.astype(jnp.float32)
    centered = samples - jnp.mean(samples, axis=1, keepdims=True)
    power = jnp.mean(centered * centered, axis=1, keepdims=True)
    factor = alive.astype(jnp.float32)[:, None] / jnp.sqrt(power + 1e-05)
    return (centered * factor).astype(jnp.bfloat16)


def correlate_kernel(live_ref, l_ref, r_ref, o_ref):
    slot = pl.program_id(0)
    length = l_ref.shape[2]

    @pl.when(live_ref[slot] > 0)
    def _():
        left = l_ref[0]
        for k in range(LAGS):
            shifted = r_ref[0, :, pl.ds(PAD - REACH + k, length)]
            summed = lax.dot_general(
                left, shifted, (((1,), (1,)), ((), ())), preferred_element_type=jnp.float32
            )
            o_ref[0, k] = (summed * (1.0 / length)).astype(o_ref.dtype)

    @pl.when(live_ref[slot] <= 0)
    def _():
        o_ref[...] = jnp.zeros(o_ref.shape, o_ref.dtype)


def correlate_all(live, left, right):
    slots, width, length = left.shape
    padded = jnp.pad(right, ((0, 0), (0, 0), (PAD, PAD)))
    out = pl.pallas_call(
        correlate_kernel,
        grid_spec=pltpu.PrefetchScalarGridSpec(
            num_scalar_prefetch=1,
            grid=(slots,),
            in_specs=[
                pl.BlockSpec((1, width, length), lambda s, lv: (s, 0, 0)),
                pl.BlockSpec((1, width, length + 2 * PAD), lambda s, lv: (s, 0, 0)),
            ],
            out_specs=pl.BlockSpec((1, LAGS, width, width), lambda s, lv: (s, 0, 0, 0)),
        ),
        out_shape=jax.ShapeDtypeStruct((slots, LAGS, width, width), jnp.bfloat16),
        compiler_params=pltpu.CompilerParams(vmem_limit_bytes=48 * 1024 * 1024),
    )(live, left, padded)
    return jnp.transpose(out, (0, 2, 1, 3))


def fetch_blocks(whitened, wanted, axis):
    n = lax.axis_size(axis)
    block, length = whitened.shape
    piece = block // n
    slots = wanted.shape[0]
    meta = jnp.zeros((piece, META), whitened.dtype).at[0, :slots].set(wanted.astype(whitened.dtype))
    pieces = jnp.concatenate(
        [whitened.reshape(n, piece, length), jnp.broadcast_to(meta, (n, piece, META))], axis=2
    )
    spread = lax.all_to_all(pieces, axis, 0, 0, tiled=True)
    asked = spread[:, 0, length:length + slots].astype(jnp.int32)
    chosen = jnp.take(spread[:, :, :length], asked, axis=0)
    arrived = lax.all_to_all(chosen, axis, 0, 0, tiled=True)
    return jnp.transpose(arrived, (1, 0, 2, 3)).reshape(slots, block, length)


def shards(traces, alive, pair_list):
    whitened = whiten(traces, alive)
    across = lax.axis_size("col")
    first = jnp.maximum(pair_list[:, 0], 0)
    second = jnp.maximum(pair_list[:, 1], 0)
    live = (pair_list[:, 0] >= 0).astype(jnp.int32)
    left = fetch_blocks(whitened, first % across, "col")
    right = fetch_blocks(whitened, second // across, "row")
    return correlate_all(live, left, right)


def solution(mesh):
    in_specs = (P(("row", "col"), None), P(("row", "col")), P(("row", "col"), None))
    out_specs = P(("row", "col"), None, None, None)
    return jax.shard_map(shards, mesh=mesh, in_specs=in_specs, out_specs=out_specs, check_vma=False)
```

```python
import jax
import jax.numpy as jnp
from jax import lax
from jax.experimental import pallas as pl
from jax.experimental.pallas import tpu as pltpu
from jax.sharding import PartitionSpec as P

LAGS = 65
REACH = (LAGS - 1) // 2
PAD = 64
META = 128


def whiten(traces, alive):
    samples = traces.astype(jnp.float32)
    centered = samples - jnp.mean(samples, axis=1, keepdims=True)
    power = jnp.mean(centered * centered, axis=1, keepdims=True)
    factor = alive.astype(jnp.float32)[:, None] / jnp.sqrt(power + 1e-05)
    return (centered * factor).astype(jnp.bfloat16)


def correlate_kernel(live_ref, l_ref, r_ref, o_ref):
    slot = pl.program_id(0)
    length = l_ref.shape[2]

    @pl.when(live_ref[slot] > 0)
    def _():
        left = l_ref[0]
        for k in range(LAGS):
            shifted = r_ref[0, pl.ds(PAD - REACH + k, length), :].astype(jnp.bfloat16)
            summed = jnp.dot(left, shifted, preferred_element_type=jnp.float32)
            o_ref[0, k] = (summed * (1.0 / length)).astype(o_ref.dtype)

    @pl.when(live_ref[slot] <= 0)
    def _():
        o_ref[...] = jnp.zeros(o_ref.shape, o_ref.dtype)


def correlate_all(live, left, right):
    slots, width, length = left.shape
    padded = jnp.pad(right, ((0, 0), (0, 0), (PAD, PAD)))
    padded = jnp.transpose(padded, (0, 2, 1)).astype(jnp.float32)
    out = pl.pallas_call(
        correlate_kernel,
        grid_spec=pltpu.PrefetchScalarGridSpec(
            num_scalar_prefetch=1,
            grid=(slots,),
            in_specs=[
                pl.BlockSpec((1, width, length), lambda s, lv: (s, 0, 0)),
                pl.BlockSpec((1, length + 2 * PAD, width), lambda s, lv: (s, 0, 0)),
            ],
            out_specs=pl.BlockSpec((1, LAGS, width, width), lambda s, lv: (s, 0, 0, 0)),
        ),
        out_shape=jax.ShapeDtypeStruct((slots, LAGS, width, width), jnp.bfloat16),
        compiler_params=pltpu.CompilerParams(vmem_limit_bytes=48 * 1024 * 1024),
    )(live, left, padded)
    return jnp.transpose(out, (0, 2, 1, 3))


def fetch_blocks(whitened, wanted, axis):
    n = lax.axis_size(axis)
    block, length = whitened.shape
    piece = block // n
    slots = wanted.shape[0]
    meta = jnp.zeros((piece, META), whitened.dtype).at[0, :slots].set(wanted.astype(whitened.dtype))
    pieces = jnp.concatenate(
        [whitened.reshape(n, piece, length), jnp.broadcast_to(meta, (n, piece, META))], axis=2
    )
    spread = lax.all_to_all(pieces, axis, 0, 0, tiled=True)
    asked = spread[:, 0, length:length + slots].astype(jnp.int32)
    chosen = jnp.take(spread[:, :, :length], asked, axis=0)
    arrived = lax.all_to_all(chosen, axis, 0, 0, tiled=True)
    return jnp.transpose(arrived, (1, 0, 2, 3)).reshape(slots, block, length)


def shards(traces, alive, pair_list):
    whitened = whiten(traces, alive)
    across = lax.axis_size("col")
    first = jnp.maximum(pair_list[:, 0], 0)
    second = jnp.maximum(pair_list[:, 1], 0)
    live = (pair_list[:, 0] >= 0).astype(jnp.int32)
    left = fetch_blocks(whitened, first % across, "col")
    right = fetch_blocks(whitened, second // across, "row")
    return correlate_all(live, left, right)


def solution(mesh):
    in_specs = (P(("row", "col"), None), P(("row", "col")), P(("row", "col"), None))
    out_specs = P(("row", "col"), None, None, None)
    return jax.shard_map(shards, mesh=mesh, in_specs=in_specs, out_specs=out_specs, check_vma=False)
```

```python
import jax
import jax.numpy as jnp
from jax import lax
from jax.experimental import pallas as pl
from jax.experimental.pallas import tpu as pltpu
from jax.sharding import PartitionSpec as P


LAGS = 65
REACH = (LAGS - 1) // 2
PAD = 64
META = 128


def whiten(traces, alive):
    samples = traces.astype(jnp.float32)
    centered = samples - jnp.mean(samples, axis=1, keepdims=True)
    power = jnp.mean(centered * centered, axis=1, keepdims=True)
    factor = alive.astype(jnp.float32)[:, None] / jnp.sqrt(power + 1e-05)
    return (centered * factor).astype(jnp.bfloat16)


def correlate_kernel(live_ref, l_ref, r_ref, o_ref):
    slot = pl.program_id(0)
    length = l_ref.shape[2]

    @pl.when(live_ref[slot] > 0)
    def _():
        left = l_ref[0]
        for k in range(LAGS):
            shifted = r_ref[0, pl.ds(PAD - REACH + k, length), :].astype(jnp.bfloat16)
            summed = jnp.dot(left, shifted, preferred_element_type=jnp.float32)
            o_ref[0, k] = (summed * (1.0 / length)).astype(o_ref.dtype)

    @pl.when(live_ref[slot] <= 0)
    def _():
        o_ref[...] = jnp.zeros(o_ref.shape, o_ref.dtype)


def correlate_all(live, left, right):
    slots, width, length = left.shape
    padded = jnp.pad(right, ((0, 0), (0, 0), (PAD, PAD)))
    padded = jnp.transpose(padded, (0, 2, 1)).astype(jnp.float32)
    out = pl.pallas_call(
        correlate_kernel,
        grid_spec=pltpu.PrefetchScalarGridSpec(
            num_scalar_prefetch=1,
            grid=(slots,),
            in_specs=[
                pl.BlockSpec((1, width, length), lambda s, lv: (s, 0, 0)),
                pl.BlockSpec((1, length + 2 * PAD, width), lambda s, lv: (s, 0, 0)),
            ],
            out_specs=pl.BlockSpec((1, LAGS, width, width), lambda s, lv: (s, 0, 0, 0)),
        ),
        out_shape=jax.ShapeDtypeStruct((slots, LAGS, width, width), jnp.bfloat16),
        compiler_params=pltpu.CompilerParams(vmem_limit_bytes=48 * 1024 * 1024),
    )(live, left, padded)
    return jnp.transpose(out, (0, 2, 1, 3))


def permute_all_to_all(chunks, axis):
    n = lax.axis_size(axis)
    me = lax.axis_index(axis)
    moved = [lax.dynamic_index_in_dim(chunks, me, 0, keepdims=False)]
    for shift in range(1, n):
        outgoing = lax.dynamic_index_in_dim(chunks, (me + shift) % n, 0, keepdims=False)
        moved.append(lax.ppermute(outgoing, axis, [(i, (i + shift) % n) for i in range(n)]))
    return jnp.take(jnp.stack(moved), (me - jnp.arange(n)) % n, axis=0)


def fetch_blocks(whitened, wanted, axis, exchange):
    n = lax.axis_size(axis)
    block, length = whitened.shape
    piece = block // n
    slots = wanted.shape[0]
    meta = jnp.zeros((piece, META), whitened.dtype).at[0, :slots].set(wanted.astype(whitened.dtype))
    pieces = jnp.concatenate(
        [whitened.reshape(n, piece, length), jnp.broadcast_to(meta, (n, piece, META))], axis=2
    )
    spread = exchange(pieces, axis)
    asked = spread[:, 0, length:length + slots].astype(jnp.int32)
    chosen = jnp.take(spread[:, :, :length], asked, axis=0)
    arrived = exchange(chosen, axis)
    return jnp.transpose(arrived, (1, 0, 2, 3)).reshape(slots, block, length)


def all_to_all(chunks, axis):
    return lax.all_to_all(chunks, axis, 0, 0, tiled=True)


def shards(traces, alive, pair_list):
    whitened = whiten(traces, alive)
    across = lax.axis_size("col")
    first = jnp.maximum(pair_list[:, 0], 0)
    second = jnp.maximum(pair_list[:, 1], 0)
    live = (pair_list[:, 0] >= 0).astype(jnp.int32)
    left = fetch_blocks(whitened, first % across, "col", all_to_all)
    right = fetch_blocks(whitened, second // across, "row", permute_all_to_all)
    return correlate_all(live, left, right)


def solution(mesh):
    in_specs = (P(("row", "col"), None), P(("row", "col")), P(("row", "col"), None))
    out_specs = P(("row", "col"), None, None, None)
    return jax.shard_map(shards, mesh=mesh, in_specs=in_specs, out_specs=out_specs, check_vma=False)
```

```python
import jax
import jax.numpy as jnp
from jax import lax
from jax.experimental import pallas as pl
from jax.experimental.pallas import tpu as pltpu
from jax.sharding import PartitionSpec as P

LAGS = 65
REACH = (LAGS - 1) // 2
PAD = 64
PAIR = 2
META = 128


def whiten(traces, alive):
    samples = traces.astype(jnp.float32)
    centered = samples - jnp.mean(samples, axis=1, keepdims=True)
    power = jnp.mean(centered * centered, axis=1, keepdims=True)
    factor = alive.astype(jnp.float32)[:, None] / jnp.sqrt(power + 1e-05)
    return (centered * factor).astype(jnp.bfloat16)


def correlate_kernel(live_ref, l_ref, r_ref, o_ref):
    slot = pl.program_id(0)
    length = l_ref.shape[2]

    @pl.when(live_ref[slot] > 0)
    def _():
        left = l_ref[0]
        width = o_ref.shape[3]
        for first in range(0, LAGS, PAIR):
            lags = range(first, min(first + PAIR, LAGS))
            shifted = jnp.concatenate(
                [r_ref[0, pl.ds(PAD - REACH + k, length), :].astype(jnp.bfloat16) for k in lags], axis=1
            )
            summed = jnp.dot(left, shifted, preferred_element_type=jnp.float32)
            summed = (summed * (1.0 / length)).astype(o_ref.dtype)
            for n, k in enumerate(lags):
                o_ref[0, k] = summed[:, n * width:(n + 1) * width]

    @pl.when(live_ref[slot] <= 0)
    def _():
        o_ref[...] = jnp.zeros(o_ref.shape, o_ref.dtype)


def correlate_all(live, left, right):
    slots, width, length = left.shape
    padded = jnp.pad(right, ((0, 0), (0, 0), (PAD, PAD)))
    padded = jnp.transpose(padded, (0, 2, 1)).astype(jnp.float32)
    out = pl.pallas_call(
        correlate_kernel,
        grid_spec=pltpu.PrefetchScalarGridSpec(
            num_scalar_prefetch=1,
            grid=(slots,),
            in_specs=[
                pl.BlockSpec((1, width, length), lambda s, lv: (s, 0, 0)),
                pl.BlockSpec((1, length + 2 * PAD, width), lambda s, lv: (s, 0, 0)),
            ],
            out_specs=pl.BlockSpec((1, LAGS, width, width), lambda s, lv: (s, 0, 0, 0)),
        ),
        out_shape=jax.ShapeDtypeStruct((slots, LAGS, width, width), jnp.bfloat16),
        compiler_params=pltpu.CompilerParams(vmem_limit_bytes=48 * 1024 * 1024),
    )(live, left, padded)
    return jnp.transpose(out, (0, 2, 1, 3))


def fetch_blocks(whitened, wanted, axis):
    n = lax.axis_size(axis)
    block, length = whitened.shape
    piece = block // n
    slots = wanted.shape[0]
    meta = jnp.zeros((piece, META), whitened.dtype).at[0, :slots].set(wanted.astype(whitened.dtype))
    pieces = jnp.concatenate(
        [whitened.reshape(n, piece, length), jnp.broadcast_to(meta, (n, piece, META))], axis=2
    )
    spread = lax.all_to_all(pieces, axis, 0, 0, tiled=True)
    asked = spread[:, 0, length:length + slots].astype(jnp.int32)
    chosen = jnp.take(spread[:, :, :length], asked, axis=0)
    arrived = lax.all_to_all(chosen, axis, 0, 0, tiled=True)
    return jnp.transpose(arrived, (1, 0, 2, 3)).reshape(slots, block, length)


def shards(traces, alive, pair_list):
    whitened = whiten(traces, alive)
    across = lax.axis_size("col")
    first = jnp.maximum(pair_list[:, 0], 0)
    second = jnp.maximum(pair_list[:, 1], 0)
    live = (pair_list[:, 0] >= 0).astype(jnp.int32)
    left = fetch_blocks(whitened, first % across, "col")
    right = fetch_blocks(whitened, second // across, "row")
    return correlate_all(live, left, right)


def solution(mesh):
    in_specs = (P(("row", "col"), None), P(("row", "col")), P(("row", "col"), None))
    out_specs = P(("row", "col"), None, None, None)
    return jax.shard_map(shards, mesh=mesh, in_specs=in_specs, out_specs=out_specs, check_vma=False)
```

```python
import jax
import jax.numpy as jnp
from jax import lax
from jax.experimental import pallas as pl
from jax.experimental.pallas import tpu as pltpu
from jax.sharding import PartitionSpec as P

LAGS = 65
REACH = (LAGS - 1) // 2
PAD = 64
PAIR = 2
META = 128


def whiten(traces, alive):
    samples = traces.astype(jnp.float32)
    centered = samples - jnp.mean(samples, axis=1, keepdims=True)
    power = jnp.mean(centered * centered, axis=1, keepdims=True)
    factor = alive.astype(jnp.float32)[:, None] / jnp.sqrt(power + 1e-05)
    return (centered * factor).astype(jnp.bfloat16)


def correlate_kernel(live_ref, l_ref, r_ref, o_ref):
    slot = pl.program_id(0)
    length = l_ref.shape[2]

    @pl.when(live_ref[slot] > 0)
    def _():
        left = l_ref[0]
        width = o_ref.shape[3]
        for first in range(0, LAGS, PAIR):
            lags = range(first, min(first + PAIR, LAGS))
            shifted = jnp.concatenate(
                [r_ref[0, pl.ds(PAD - REACH + k, length), :].astype(jnp.bfloat16) for k in lags], axis=1
            )
            summed = jnp.dot(left, shifted, preferred_element_type=jnp.float32)
            summed = (summed * (1.0 / length)).astype(o_ref.dtype)
            for n, k in enumerate(lags):
                o_ref[0, k] = summed[:, n * width:(n + 1) * width]

    @pl.when(live_ref[slot] <= 0)
    def _():
        o_ref[...] = jnp.zeros(o_ref.shape, o_ref.dtype)


def correlate_all(live, left, right):
    slots, width, length = left.shape
    padded = jnp.pad(right, ((0, 0), (0, 0), (PAD, PAD)))
    padded = jnp.transpose(padded, (0, 2, 1)).astype(jnp.float32)
    out = pl.pallas_call(
        correlate_kernel,
        grid_spec=pltpu.PrefetchScalarGridSpec(
            num_scalar_prefetch=1,
            grid=(slots,),
            in_specs=[
                pl.BlockSpec((1, width, length), lambda s, lv: (s, 0, 0)),
                pl.BlockSpec((1, length + 2 * PAD, width), lambda s, lv: (s, 0, 0)),
            ],
            out_specs=pl.BlockSpec((1, LAGS, width, width), lambda s, lv: (s, 0, 0, 0)),
        ),
        out_shape=jax.ShapeDtypeStruct((slots, LAGS, width, width), jnp.bfloat16),
        compiler_params=pltpu.CompilerParams(vmem_limit_bytes=48 * 1024 * 1024),
    )(live, left, padded)
    return jnp.transpose(out, (0, 2, 1, 3))


def prepare_kernel(pairs_ref, traces_ref, alive_ref, col_ref, row_ref):
    pieces, piece, width = col_ref.shape
    length = traces_ref.shape[1]
    slots = pairs_ref.shape[0]
    samples = traces_ref[...].astype(jnp.float32)
    centered = samples - jnp.mean(samples, axis=1, keepdims=True)
    power = jnp.mean(centered * centered, axis=1, keepdims=True)
    channels = samples.shape[0]
    alive = jnp.transpose(jnp.broadcast_to(alive_ref[...].astype(jnp.float32), (channels, channels)))[:, :1]
    whitened = centered * (alive / jnp.sqrt(power + 1e-05))
    sublane = lax.broadcasted_iota(jnp.int32, (piece, width - length), 0)
    lane = lax.broadcasted_iota(jnp.int32, (piece, width - length), 1)
    col_meta = jnp.zeros((piece, width - length), jnp.float32)
    row_meta = jnp.zeros((piece, width - length), jnp.float32)
    for s in range(slots):
        at = (sublane == 0) & (lane == s)
        col_meta = jnp.where(at, (jnp.maximum(pairs_ref[s, 0], 0) % pieces).astype(jnp.float32), col_meta)
        row_meta = jnp.where(at, (jnp.maximum(pairs_ref[s, 1], 0) // pieces).astype(jnp.float32), row_meta)
    for p in range(pieces):
        rows = whitened[p * piece:(p + 1) * piece].astype(col_ref.dtype)
        col_ref[p, :, :length] = rows
        row_ref[p, :, :length] = rows
        col_ref[p, :, length:] = col_meta.astype(col_ref.dtype)
        row_ref[p, :, length:] = row_meta.astype(row_ref.dtype)


def prepare(traces, alive, pair_list, pieces):
    channels, length = traces.shape
    shape = jax.ShapeDtypeStruct((pieces, channels // pieces, length + META), jnp.bfloat16)
    return pl.pallas_call(
        prepare_kernel,
        grid_spec=pltpu.PrefetchScalarGridSpec(
            num_scalar_prefetch=1,
            grid=(),
            in_specs=[
                pl.BlockSpec((channels, length), lambda pr: (0, 0)),
                pl.BlockSpec((1, channels), lambda pr: (0, 0)),
            ],
            out_specs=[
                pl.BlockSpec(shape.shape, lambda pr: (0, 0, 0)),
                pl.BlockSpec(shape.shape, lambda pr: (0, 0, 0)),
            ],
        ),
        out_shape=[shape, shape],
    )(pair_list, traces, alive.reshape(1, channels))


def fetch_blocks(pieces, axis, slots):
    n, piece, width = pieces.shape
    length = width - META
    spread = lax.all_to_all(pieces, axis, 0, 0, tiled=True)
    asked = spread[:, 0, length:length + slots].astype(jnp.int32)
    chosen = jnp.take(spread[:, :, :length], asked, axis=0)
    arrived = lax.all_to_all(chosen, axis, 0, 0, tiled=True)
    return jnp.transpose(arrived, (1, 0, 2, 3)).reshape(slots, n * piece, length)


def shards(traces, alive, pair_list):
    across = lax.axis_size("col")
    slots = pair_list.shape[0]
    col_pieces, row_pieces = prepare(traces, alive, pair_list, across)
    live = (pair_list[:, 0] >= 0).astype(jnp.int32)
    left = fetch_blocks(col_pieces, "col", slots)
    right = fetch_blocks(row_pieces, "row", slots)
    return correlate_all(live, left, right)


def solution(mesh):
    in_specs = (P(("row", "col"), None), P(("row", "col")), P(("row", "col"), None))
    out_specs = P(("row", "col"), None, None, None)
    return jax.shard_map(shards, mesh=mesh, in_specs=in_specs, out_specs=out_specs, check_vma=False)
```

```python
import jax
import jax.numpy as jnp
from jax import lax
from jax.experimental import pallas as pl
from jax.experimental.pallas import tpu as pltpu
from jax.sharding import PartitionSpec as P

LAGS = 65
REACH = (LAGS - 1) // 2
PAD = 64
PAIR = 2
META = 128


def whiten(traces, alive):
    samples = traces.astype(jnp.float32)
    centered = samples - jnp.mean(samples, axis=1, keepdims=True)
    power = jnp.mean(centered * centered, axis=1, keepdims=True)
    factor = alive.astype(jnp.float32)[:, None] / jnp.sqrt(power + 1e-05)
    return (centered * factor).astype(jnp.bfloat16)


def correlate_kernel(live_ref, l_ref, r_ref, o_ref):
    slot = pl.program_id(0)
    length = l_ref.shape[2]

    @pl.when(live_ref[slot] > 0)
    def _():
        left = l_ref[0]
        width = o_ref.shape[3]
        for first in range(0, LAGS, PAIR):
            lags = range(first, min(first + PAIR, LAGS))
            shifted = jnp.concatenate(
                [r_ref[0, pl.ds(PAD - REACH + k, length), :].astype(jnp.bfloat16) for k in lags], axis=1
            )
            summed = jnp.dot(left, shifted, preferred_element_type=jnp.float32)
            summed = (summed * (1.0 / length)).astype(o_ref.dtype)
            for n, k in enumerate(lags):
                o_ref[0, k] = summed[:, n * width:(n + 1) * width]

    @pl.when(live_ref[slot] <= 0)
    def _():
        o_ref[...] = jnp.zeros(o_ref.shape, o_ref.dtype)


def correlate_all(live, left, right):
    slots, width, length = left.shape
    padded = jnp.pad(right, ((0, 0), (0, 0), (PAD, PAD)))
    padded = jnp.transpose(padded, (0, 2, 1)).astype(jnp.float32)
    out = pl.pallas_call(
        correlate_kernel,
        grid_spec=pltpu.PrefetchScalarGridSpec(
            num_scalar_prefetch=1,
            grid=(slots,),
            in_specs=[
                pl.BlockSpec((1, width, length), lambda s, lv: (s, 0, 0)),
                pl.BlockSpec((1, length + 2 * PAD, width), lambda s, lv: (s, 0, 0)),
            ],
            out_specs=pl.BlockSpec((1, LAGS, width, width), lambda s, lv: (s, 0, 0, 0)),
        ),
        out_shape=jax.ShapeDtypeStruct((slots, LAGS, width, width), jnp.bfloat16),
        compiler_params=pltpu.CompilerParams(vmem_limit_bytes=48 * 1024 * 1024),
    )(live, left, padded)
    return jnp.transpose(out, (0, 2, 1, 3))


def prepare_kernel(pairs_ref, traces_ref, alive_ref, col_ref, row_ref):
    pieces, piece, width = col_ref.shape
    length = traces_ref.shape[1]
    slots = pairs_ref.shape[1]
    samples = traces_ref[...].astype(jnp.float32)
    centered = samples - jnp.mean(samples, axis=1, keepdims=True)
    power = jnp.mean(centered * centered, axis=1, keepdims=True)
    channels = samples.shape[0]
    alive = jnp.transpose(jnp.broadcast_to(alive_ref[...].astype(jnp.float32), (channels, channels)))[:, :1]
    whitened = centered * (alive / jnp.sqrt(power + 1e-05))
    sublane = lax.broadcasted_iota(jnp.int32, (piece, width - length), 0)
    lane = lax.broadcasted_iota(jnp.int32, (piece, width - length), 1)
    col_meta = jnp.zeros((piece, width - length), jnp.float32)
    row_meta = jnp.zeros((piece, width - length), jnp.float32)
    for s in range(slots):
        at = (sublane == 0) & (lane == s)
        col_meta = jnp.where(at, (jnp.maximum(pairs_ref[0, s], 0) % pieces).astype(jnp.float32), col_meta)
        row_meta = jnp.where(at, (jnp.maximum(pairs_ref[1, s], 0) // pieces).astype(jnp.float32), row_meta)
    for p in range(pieces):
        rows = whitened[p * piece:(p + 1) * piece].astype(col_ref.dtype)
        col_ref[p, :, :length] = rows
        row_ref[p, :, :length] = rows
        col_ref[p, :, length:] = col_meta.astype(col_ref.dtype)
        row_ref[p, :, length:] = row_meta.astype(row_ref.dtype)


def prepare(traces, alive, pair_list, pieces):
    channels, length = traces.shape
    shape = jax.ShapeDtypeStruct((pieces, channels // pieces, length + META), jnp.bfloat16)
    return pl.pallas_call(
        prepare_kernel,
        grid_spec=pltpu.PrefetchScalarGridSpec(
            num_scalar_prefetch=1,
            grid=(),
            in_specs=[
                pl.BlockSpec((channels, length), lambda pr: (0, 0)),
                pl.BlockSpec((1, channels), lambda pr: (0, 0)),
            ],
            out_specs=[
                pl.BlockSpec(shape.shape, lambda pr: (0, 0, 0)),
                pl.BlockSpec(shape.shape, lambda pr: (0, 0, 0)),
            ],
        ),
        out_shape=[shape, shape],
    )(pair_list.T, traces, alive.reshape(1, channels))


def fetch_blocks(pieces, axis, slots):
    n, piece, width = pieces.shape
    length = width - META
    spread = lax.all_to_all(pieces, axis, 0, 0, tiled=True)
    asked = spread[:, 0, length:length + slots].astype(jnp.int32)
    chosen = jnp.take(spread[:, :, :length], asked, axis=0)
    arrived = lax.all_to_all(chosen, axis, 0, 0, tiled=True)
    return jnp.transpose(arrived, (1, 0, 2, 3)).reshape(slots, n * piece, length)


def shards(traces, alive, pair_list):
    across = lax.axis_size("col")
    slots = pair_list.shape[0]
    col_pieces, row_pieces = prepare(traces, alive, pair_list, across)
    live = (pair_list[:, 0] >= 0).astype(jnp.int32)
    left = fetch_blocks(col_pieces, "col", slots)
    right = fetch_blocks(row_pieces, "row", slots)
    return correlate_all(live, left, right)


def solution(mesh):
    in_specs = (P(("row", "col"), None), P(("row", "col")), P(("row", "col"), None))
    out_specs = P(("row", "col"), None, None, None)
    return jax.shard_map(shards, mesh=mesh, in_specs=in_specs, out_specs=out_specs, check_vma=False)
```

```python
import jax
import jax.numpy as jnp
from jax import lax
from jax.experimental import pallas as pl
from jax.experimental.pallas import tpu as pltpu
from jax.sharding import PartitionSpec as P

LAGS = 65
REACH = (LAGS - 1) // 2
PAD = 64
PAIR = 2
META = 128


def whiten(traces, alive):
    samples = traces.astype(jnp.float32)
    centered = samples - jnp.mean(samples, axis=1, keepdims=True)
    power = jnp.mean(centered * centered, axis=1, keepdims=True)
    factor = alive.astype(jnp.float32)[:, None] / jnp.sqrt(power + 1e-05)
    return (centered * factor).astype(jnp.bfloat16)


def correlate_kernel(live_ref, l_ref, r_ref, o_ref):
    slot = pl.program_id(0)
    length = l_ref.shape[2]

    @pl.when(live_ref[slot] > 0)
    def _():
        left = l_ref[0]
        width = o_ref.shape[3]
        for first in range(0, LAGS, PAIR):
            lags = range(first, min(first + PAIR, LAGS))
            shifted = jnp.concatenate(
                [r_ref[0, pl.ds(PAD - REACH + k, length), :] for k in lags], axis=1
            )
            summed = jnp.dot(left, shifted, preferred_element_type=jnp.float32)
            summed = (summed * (1.0 / length)).astype(o_ref.dtype)
            for n, k in enumerate(lags):
                o_ref[0, k] = summed[:, n * width:(n + 1) * width]

    @pl.when(live_ref[slot] <= 0)
    def _():
        o_ref[...] = jnp.zeros(o_ref.shape, o_ref.dtype)


def correlate_all(live, left, right):
    slots, width, length = left.shape
    padded = jnp.pad(right, ((0, 0), (0, 0), (PAD, PAD)))
    padded = jnp.transpose(padded, (0, 2, 1))
    out = pl.pallas_call(
        correlate_kernel,
        grid_spec=pltpu.PrefetchScalarGridSpec(
            num_scalar_prefetch=1,
            grid=(slots,),
            in_specs=[
                pl.BlockSpec((1, width, length), lambda s, lv: (s, 0, 0)),
                pl.BlockSpec((1, length + 2 * PAD, width), lambda s, lv: (s, 0, 0)),
            ],
            out_specs=pl.BlockSpec((1, LAGS, width, width), lambda s, lv: (s, 0, 0, 0)),
        ),
        out_shape=jax.ShapeDtypeStruct((slots, LAGS, width, width), jnp.bfloat16),
        compiler_params=pltpu.CompilerParams(vmem_limit_bytes=48 * 1024 * 1024),
    )(live, left, padded)
    return jnp.transpose(out, (0, 2, 1, 3))


def prepare_kernel(pairs_ref, traces_ref, alive_ref, col_ref, row_ref):
    pieces, piece, width = col_ref.shape
    length = traces_ref.shape[1]
    slots = pairs_ref.shape[1]
    samples = traces_ref[...].astype(jnp.float32)
    centered = samples - jnp.mean(samples, axis=1, keepdims=True)
    power = jnp.mean(centered * centered, axis=1, keepdims=True)
    channels = samples.shape[0]
    alive = jnp.transpose(jnp.broadcast_to(alive_ref[...].astype(jnp.float32), (channels, channels)))[:, :1]
    whitened = centered * (alive / jnp.sqrt(power + 1e-05))
    sublane = lax.broadcasted_iota(jnp.int32, (piece, width - length), 0)
    lane = lax.broadcasted_iota(jnp.int32, (piece, width - length), 1)
    col_meta = jnp.zeros((piece, width - length), jnp.float32)
    row_meta = jnp.zeros((piece, width - length), jnp.float32)
    for s in range(slots):
        at = (sublane == 0) & (lane == s)
        col_meta = jnp.where(at, (jnp.maximum(pairs_ref[0, s], 0) % pieces).astype(jnp.float32), col_meta)
        row_meta = jnp.where(at, (jnp.maximum(pairs_ref[1, s], 0) // pieces).astype(jnp.float32), row_meta)
    for p in range(pieces):
        rows = whitened[p * piece:(p + 1) * piece].astype(col_ref.dtype)
        col_ref[p, :, :length] = rows
        row_ref[p, :, :length] = rows
        col_ref[p, :, length:] = col_meta.astype(col_ref.dtype)
        row_ref[p, :, length:] = row_meta.astype(row_ref.dtype)


def prepare(traces, alive, pair_list, pieces):
    channels, length = traces.shape
    shape = jax.ShapeDtypeStruct((pieces, channels // pieces, length + META), jnp.bfloat16)
    return pl.pallas_call(
        prepare_kernel,
        grid_spec=pltpu.PrefetchScalarGridSpec(
            num_scalar_prefetch=1,
            grid=(),
            in_specs=[
                pl.BlockSpec((channels, length), lambda pr: (0, 0)),
                pl.BlockSpec((1, channels), lambda pr: (0, 0)),
            ],
            out_specs=[
                pl.BlockSpec(shape.shape, lambda pr: (0, 0, 0)),
                pl.BlockSpec(shape.shape, lambda pr: (0, 0, 0)),
            ],
        ),
        out_shape=[shape, shape],
    )(pair_list.T, traces, alive.reshape(1, channels))


def fetch_blocks(pieces, axis, slots):
    n, piece, width = pieces.shape
    length = width - META
    spread = lax.all_to_all(pieces, axis, 0, 0, tiled=True)
    asked = spread[:, 0, length:length + slots].astype(jnp.int32)
    chosen = jnp.take(spread[:, :, :length], asked, axis=0)
    arrived = lax.all_to_all(chosen, axis, 0, 0, tiled=True)
    return jnp.transpose(arrived, (1, 0, 2, 3)).reshape(slots, n * piece, length)


def shards(traces, alive, pair_list):
    across = lax.axis_size("col")
    slots = pair_list.shape[0]
    col_pieces, row_pieces = prepare(traces, alive, pair_list, across)
    live = (pair_list[:, 0] >= 0).astype(jnp.int32)
    left = fetch_blocks(col_pieces, "col", slots)
    right = fetch_blocks(row_pieces, "row", slots)
    return correlate_all(live, left, right)


def solution(mesh):
    in_specs = (P(("row", "col"), None), P(("row", "col")), P(("row", "col"), None))
    out_specs = P(("row", "col"), None, None, None)
    return jax.shard_map(shards, mesh=mesh, in_specs=in_specs, out_specs=out_specs, check_vma=False)
```

```python
import jax
import jax.numpy as jnp
from jax import lax
from jax.experimental import pallas as pl
from jax.experimental.pallas import tpu as pltpu
from jax.sharding import PartitionSpec as P

LAGS = 65
REACH = (LAGS - 1) // 2
PAD = 64
PAIR = 2
META = 128


def whiten(traces, alive):
    samples = traces.astype(jnp.float32)
    centered = samples - jnp.mean(samples, axis=1, keepdims=True)
    power = jnp.mean(centered * centered, axis=1, keepdims=True)
    factor = alive.astype(jnp.float32)[:, None] / jnp.sqrt(power + 1e-05)
    return (centered * factor).astype(jnp.bfloat16)


def correlate_kernel(live_ref, l_ref, r_ref, o_ref):
    slot = pl.program_id(0)
    length = l_ref.shape[2]

    @pl.when(live_ref[slot] > 0)
    def _():
        left = l_ref[0]
        width = o_ref.shape[3]
        for first in range(0, LAGS, PAIR):
            lags = range(first, min(first + PAIR, LAGS))
            shifted = jnp.concatenate(
                [r_ref[0, pl.ds(PAD - REACH + k, length), :] for k in lags], axis=1
            )
            summed = jnp.dot(left, shifted, preferred_element_type=jnp.float32)
            summed = (summed * (1.0 / length)).astype(o_ref.dtype)
            for n, k in enumerate(lags):
                o_ref[0, k] = summed[:, n * width:(n + 1) * width]

    @pl.when(live_ref[slot] <= 0)
    def _():
        o_ref[...] = jnp.zeros(o_ref.shape, o_ref.dtype)


def correlate_all(live, left, right):
    slots, width, length = left.shape
    padded = jnp.pad(right, ((0, 0), (0, 0), (PAD, PAD)))
    padded = jnp.transpose(padded, (0, 2, 1))
    out = pl.pallas_call(
        correlate_kernel,
        grid_spec=pltpu.PrefetchScalarGridSpec(
            num_scalar_prefetch=1,
            grid=(slots,),
            in_specs=[
                pl.BlockSpec((1, width, length), lambda s, lv: (s, 0, 0)),
                pl.BlockSpec((1, length + 2 * PAD, width), lambda s, lv: (s, 0, 0)),
            ],
            out_specs=pl.BlockSpec((1, LAGS, width, width), lambda s, lv: (s, 0, 0, 0)),
        ),
        out_shape=jax.ShapeDtypeStruct((slots, LAGS, width, width), jnp.bfloat16),
        compiler_params=pltpu.CompilerParams(vmem_limit_bytes=48 * 1024 * 1024),
    )(live, left, padded)
    return jnp.transpose(out, (0, 2, 1, 3))


def prepare_kernel(pairs_ref, traces_ref, alive_ref, row_ref):
    pieces, piece, width = row_ref.shape
    length = traces_ref.shape[1]
    slots = pairs_ref.shape[1]
    samples = traces_ref[...].astype(jnp.float32)
    centered = samples - jnp.mean(samples, axis=1, keepdims=True)
    power = jnp.mean(centered * centered, axis=1, keepdims=True)
    channels = samples.shape[0]
    alive = jnp.transpose(jnp.broadcast_to(alive_ref[...].astype(jnp.float32), (channels, channels)))[:, :1]
    whitened = centered * (alive / jnp.sqrt(power + 1e-05))
    sublane = lax.broadcasted_iota(jnp.int32, (piece, width - length), 0)
    lane = lax.broadcasted_iota(jnp.int32, (piece, width - length), 1)
    row_meta = jnp.zeros((piece, width - length), jnp.float32)
    for s in range(slots):
        at = (sublane == 0) & (lane == s)
        row_meta = jnp.where(at, (jnp.maximum(pairs_ref[1, s], 0) // pieces).astype(jnp.float32), row_meta)
    for p in range(pieces):
        row_ref[p, :, :length] = whitened[p * piece:(p + 1) * piece].astype(row_ref.dtype)
        row_ref[p, :, length:] = row_meta.astype(row_ref.dtype)


def prepare(traces, alive, pair_list, pieces):
    channels, length = traces.shape
    shape = jax.ShapeDtypeStruct((pieces, channels // pieces, length + META), jnp.bfloat16)
    pieces_out = pl.pallas_call(
        prepare_kernel,
        grid_spec=pltpu.PrefetchScalarGridSpec(
            num_scalar_prefetch=1,
            grid=(),
            in_specs=[
                pl.BlockSpec((channels, length), lambda pr: (0, 0)),
                pl.BlockSpec((1, channels), lambda pr: (0, 0)),
            ],
            out_specs=pl.BlockSpec(shape.shape, lambda pr: (0, 0, 0)),
        ),
        out_shape=shape,
    )(pair_list.T, traces, alive.reshape(1, channels))
    row_pieces = pieces_out
    slots = pair_list.shape[0]
    wanted = (jnp.maximum(pair_list[:, 0], 0) % pieces).astype(row_pieces.dtype)
    meta = jnp.zeros((row_pieces.shape[1], META), row_pieces.dtype).at[0, :slots].set(wanted)
    col_pieces = jnp.concatenate(
        [row_pieces[:, :, :length], jnp.broadcast_to(meta, (pieces,) + meta.shape)], axis=2
    )
    return col_pieces, row_pieces


def fetch_blocks(pieces, axis, slots):
    n, piece, width = pieces.shape
    length = width - META
    spread = lax.all_to_all(pieces, axis, 0, 0, tiled=True)
    asked = spread[:, 0, length:length + slots].astype(jnp.int32)
    chosen = jnp.take(spread[:, :, :length], asked, axis=0)
    arrived = lax.all_to_all(chosen, axis, 0, 0, tiled=True)
    return jnp.transpose(arrived, (1, 0, 2, 3)).reshape(slots, n * piece, length)


def shards(traces, alive, pair_list):
    across = lax.axis_size("col")
    slots = pair_list.shape[0]
    col_pieces, row_pieces = prepare(traces, alive, pair_list, across)
    live = (pair_list[:, 0] >= 0).astype(jnp.int32)
    left = fetch_blocks(col_pieces, "col", slots)
    right = fetch_blocks(row_pieces, "row", slots)
    return correlate_all(live, left, right)


def solution(mesh):
    in_specs = (P(("row", "col"), None), P(("row", "col")), P(("row", "col"), None))
    out_specs = P(("row", "col"), None, None, None)
    return jax.shard_map(shards, mesh=mesh, in_specs=in_specs, out_specs=out_specs, check_vma=False)
```

```python
import jax
import jax.numpy as jnp
from jax import lax
from jax.experimental import pallas as pl
from jax.experimental.pallas import tpu as pltpu
from jax.sharding import PartitionSpec as P

LAGS = 65
REACH = (LAGS - 1) // 2
PAD = 64
PAIR = 2
META = 128


def whiten(traces, alive):
    samples = traces.astype(jnp.float32)
    centered = samples - jnp.mean(samples, axis=1, keepdims=True)
    power = jnp.mean(centered * centered, axis=1, keepdims=True)
    factor = alive.astype(jnp.float32)[:, None] / jnp.sqrt(power + 1e-05)
    return (centered * factor).astype(jnp.bfloat16)


def correlate_kernel(live_ref, l_ref, r_ref, o_ref):
    slot = pl.program_id(0)
    length = l_ref.shape[2]

    @pl.when(live_ref[slot] > 0)
    def _():
        left = l_ref[0]
        width = o_ref.shape[3]
        for first in range(0, LAGS, PAIR):
            lags = range(first, min(first + PAIR, LAGS))
            shifted = jnp.concatenate(
                [r_ref[0, pl.ds(PAD - REACH + k, length), :] for k in lags], axis=1
            )
            summed = jnp.dot(left, shifted, preferred_element_type=jnp.float32)
            summed = (summed * (1.0 / length)).astype(o_ref.dtype)
            for n, k in enumerate(lags):
                o_ref[0, k] = summed[:, n * width:(n + 1) * width]

    @pl.when(live_ref[slot] <= 0)
    def _():
        o_ref[...] = jnp.zeros(o_ref.shape, o_ref.dtype)


def correlate_all(live, left, right):
    slots, width, length = left.shape
    padded = jnp.pad(right, ((0, 0), (0, 0), (PAD, PAD)))
    padded = jnp.transpose(padded, (0, 2, 1))
    out = pl.pallas_call(
        correlate_kernel,
        grid_spec=pltpu.PrefetchScalarGridSpec(
            num_scalar_prefetch=1,
            grid=(slots,),
            in_specs=[
                pl.BlockSpec((1, width, length), lambda s, lv: (s, 0, 0)),
                pl.BlockSpec((1, length + 2 * PAD, width), lambda s, lv: (s, 0, 0)),
            ],
            out_specs=pl.BlockSpec((1, LAGS, width, width), lambda s, lv: (s, 0, 0, 0)),
        ),
        out_shape=jax.ShapeDtypeStruct((slots, LAGS, width, width), jnp.bfloat16),
        compiler_params=pltpu.CompilerParams(vmem_limit_bytes=48 * 1024 * 1024),
    )(live, left, padded)
    return jnp.transpose(out, (0, 2, 1, 3))


def prepare_kernel(pairs_ref, traces_ref, alive_ref, row_ref):
    pieces, piece, width = row_ref.shape
    length = traces_ref.shape[1]
    slots = pairs_ref.shape[1]
    samples = traces_ref[...].astype(jnp.float32)
    centered = samples - jnp.mean(samples, axis=1, keepdims=True)
    power = jnp.mean(centered * centered, axis=1, keepdims=True)
    channels = samples.shape[0]
    alive = jnp.transpose(jnp.broadcast_to(alive_ref[...].astype(jnp.float32), (channels, channels)))[:, :1]
    whitened = centered * (alive / jnp.sqrt(power + 1e-05))
    sublane = lax.broadcasted_iota(jnp.int32, (piece, width - length), 0)
    lane = lax.broadcasted_iota(jnp.int32, (piece, width - length), 1)
    row_meta = jnp.zeros((piece, width - length), jnp.float32)
    for s in range(slots):
        at = (sublane == 0) & (lane == s)
        row_meta = jnp.where(at, (jnp.maximum(pairs_ref[1, s], 0) // pieces).astype(jnp.float32), row_meta)
    for p in range(pieces):
        row_ref[p, :, :length] = whitened[p * piece:(p + 1) * piece].astype(row_ref.dtype)
        row_ref[p, :, length:] = row_meta.astype(row_ref.dtype)


def prepare(traces, alive, pair_list, pieces):
    channels, length = traces.shape
    shape = jax.ShapeDtypeStruct((pieces, channels // pieces, length + META), jnp.bfloat16)
    pieces_out = pl.pallas_call(
        prepare_kernel,
        grid_spec=pltpu.PrefetchScalarGridSpec(
            num_scalar_prefetch=1,
            grid=(),
            in_specs=[
                pl.BlockSpec((channels, length), lambda pr: (0, 0)),
                pl.BlockSpec((1, channels), lambda pr: (0, 0)),
            ],
            out_specs=pl.BlockSpec(shape.shape, lambda pr: (0, 0, 0)),
        ),
        out_shape=shape,
    )(pair_list.T, traces, alive.reshape(1, channels))
    row_pieces = pieces_out
    slots = pair_list.shape[0]
    wanted = (jnp.maximum(pair_list[:, 0], 0) % pieces).astype(row_pieces.dtype)
    meta = jnp.zeros((row_pieces.shape[1], META), row_pieces.dtype).at[0, :slots].set(wanted)
    col_pieces = jnp.concatenate(
        [row_pieces[:, :, :length], jnp.broadcast_to(meta, (pieces,) + meta.shape)], axis=2
    )
    return col_pieces, row_pieces


def fetch_blocks(pieces, axis, slots):
    n, piece, width = pieces.shape
    length = width - META
    spread = lax.all_to_all(pieces, axis, 0, 0, tiled=True)
    asked = spread[:, 0, length:length + slots].astype(jnp.int32)
    chosen = jnp.take(spread[:, :, :length], asked, axis=0, mode="clip")
    arrived = lax.all_to_all(chosen, axis, 0, 0, tiled=True)
    return jnp.transpose(arrived, (1, 0, 2, 3)).reshape(slots, n * piece, length)


def shards(traces, alive, pair_list):
    across = lax.axis_size("col")
    slots = pair_list.shape[0]
    col_pieces, row_pieces = prepare(traces, alive, pair_list, across)
    live = (pair_list[:, 0] >= 0).astype(jnp.int32)
    left = fetch_blocks(col_pieces, "col", slots)
    right = fetch_blocks(row_pieces, "row", slots)
    return correlate_all(live, left, right)


def solution(mesh):
    in_specs = (P(("row", "col"), None), P(("row", "col")), P(("row", "col"), None))
    out_specs = P(("row", "col"), None, None, None)
    return jax.shard_map(shards, mesh=mesh, in_specs=in_specs, out_specs=out_specs, check_vma=False)
```
